256 devices in a mesh: blk: 64 (over z, x, core), req: 4 (over y).
Axes of the slice: x: 4, y: 4, z: 8, core: 2. Of those that a mesh axis runs over, the one named last changes fastest.
Arguments:
- tokens: bfloat16 [32, 4, 2048], P('req'), may hold values from -6 to 6
- lengths: int32 [32], replicated, may hold values from 1 to 8192, 104857 in all
- slot_request: int32 [32], replicated, may hold values from 0 to 31, each once
- ln1_gain: float32 [2048], replicated, may hold values from 0.5 to 1.5
- ln1_bias: float32 [2048], replicated, may hold values from -3 to 3
- w_query: bfloat16 [2048, 2048], P(None, 'blk'), may hold values from -0.125 to 0.125
- w_key: bfloat16 [2048, 2048], P(None, 'blk'), may hold values from -0.125 to 0.125
- w_value: bfloat16 [2048, 2048], P(None, 'blk'), may hold values from -0.125 to 0.125
- b_query: float32 [2048], P('blk'), may hold values from -3 to 3
- b_key: float32 [2048], P('blk'), may hold values from -3 to 3
- b_value: float32 [2048], P('blk'), may hold values from -3 to 3
- cache_keys: bfloat16 [32, 8192, 2048], P('req', 'blk'), may hold values from -500 to 500
- cache_values: bfloat16 [32, 8192, 2048], P('req', 'blk'), may hold values from -9 to 9
- w_out: bfloat16 [2048, 2048], P(None, 'blk'), may hold values from -0.125 to 0.125
- ln2_gain: float32 [2048], replicated, may hold values from 0.5 to 1.5
- ln2_bias: float32 [2048], replicated, may hold values from -3 to 3
- w_gate: bfloat16 [2048, 5632], P(None, 'blk'), may hold values from -0.125 to 0.125
- w_up: bfloat16 [2048, 5632], P(None, 'blk'), may hold values from -0.125 to 0.125
- w_down: bfloat16 [5632, 2048], P('blk'), may hold values from -0.078125 to 0.078125
Outputs:
- layer_out: bfloat16 [32, 4, 2048], P('req', None, 'blk')
- new_keys: bfloat16 [32, 4, 2048], P('req', None, 'blk')
- new_values: bfloat16 [32, 4, 2048], P('req', None, 'blk')
The draws below stay inside these ranges and needn't reach their ends.
Inputs may be any that keep to these rules, and one draw needn't show every extreme that they name: `lengths`: every request has 1 or more cached tokens; some request has exactly 8192. A permutation of the 32 requests: cache slot i holds request slot_request[i].
All inputs are finite; a program needn't handle non-finite values.
Results may differ from the reference program's by a relative error of at most 0.012.
The reference program's roundings to bfloat16 on the way count: a program that leaves them out, or rounds other values in their place, can miss the bound.
Values may be sent and summed in bfloat16 or wider, within the bound.
No kernel may reach another device: no remote copies, remote signals or barrier semaphores. Data moves between devices by JAX's collectives and lax.ppermute only.
A program may use at most 192 MiB of HBM per device.

```python
import math
import jax
import jax.numpy as jnp
import numpy as np
from jax import lax

D = 2048
HEADS = 32
FF = 5632
HEAD_DIM = 64
ROT = 16
NEW = 4
BLK_LEN = 128
REQS = 32
SEQ = 8192
N_BLK = 64


def draw_cache_keys(key, part):
    full_shape = (REQS, SEQ, D)
    return (1.5 * jax.random.truncated_normal(key, -6.0, 6.0, full_shape, jnp.float32)).astype(jnp.bfloat16)


def bias_pair(key):
    base_key = jax.random.fold_in(key, 4099)
    head_key, common_key, query_key, key_key = jax.random.split(base_key, 4)
    head_shape = (HEADS, HEAD_DIM)
    amplitude = jnp.exp(jax.random.uniform(head_key, (HEADS, 1), jnp.float32, -1.204, 0.5878))
    common = jax.random.normal(common_key, head_shape, jnp.float32)
    query_own = 0.3 * jax.random.normal(query_key, head_shape, jnp.float32)
    key_own = 0.3 * jax.random.normal(key_key, head_shape, jnp.float32)
    query_bias = jnp.clip(amplitude * (common + query_own), -3.0, 3.0).reshape(D)
    key_bias = jnp.clip(amplitude * (common + key_own), -3.0, 3.0).reshape(D)
    return (query_bias, key_bias)


def draw_b_query(key, part):
    return bias_pair(key)[0]


def draw_b_key(key, part):
    return bias_pair(key)[1]


def block_scale(own_key, dims, cuts, low, largest):
    factor_of, own = 1.0, jax.random.fold_in(own_key, 6)
    for axis_at, shards_of in cuts:
        steps = jnp.exp(jax.random.uniform(jax.random.fold_in(own, axis_at), (shards_of,), jnp.float32, low / len(cuts), largest / len(cuts)))
        factor_of = factor_of * jnp.repeat(steps, dims[axis_at] // shards_of).reshape([-1 if axis == axis_at else 1 for axis in range(len(dims))])
    return factor_of


def length_profile(number_of, total, limit, skew):
    portions = [(1 << 20) // math.isqrt(standing ** skew) + 1 for standing in range(2, number_of + 1)]
    surplus, counts = total - limit - (number_of - 1), [1] * (number_of - 1)
    while surplus > 0:
        movable = [i for i in range(number_of - 1) if counts[i] < limit]
        mass, budget = sum([portions[i] for i in movable]), surplus
        for i in movable:
            extra = min(limit - counts[i], max(1, budget * portions[i] // mass), surplus)
            counts[i] = counts[i] + extra
            surplus = surplus - extra
    return np.array([limit] + counts)


def ragged(key, number_of, total, reach, lean):
    if number_of == 2:
        one = jax.random.randint(key, (), max(1, total - reach), min(reach, total - 1) + 1)
        return jnp.stack([one, total - one])
    tallies = jnp.asarray(length_profile(number_of, total, reach, lean), jnp.int32)
    pairs = (number_of - 1) // 2
    donor, sink = tallies[1:1 + 2 * pairs:2], tallies[2:2 + 2 * pairs:2]
    margin = jnp.minimum(donor - 1, reach - sink)
    passed = jax.random.randint(jax.random.fold_in(key, 1), (pairs,), 0, 1 << 20) % (margin + 1)
    tallies = tallies.at[1:1 + 2 * pairs:2].set(donor - passed).at[2:2 + 2 * pairs:2].set(sink + passed)
    return tallies[jax.random.permutation(jax.random.fold_in(key, 2), number_of)]


def gaussian(own_key, extent, width, reach, shards=(), kind=jnp.bfloat16):
    gain = block_scale(own_key, extent, shards, -0.22, 0.18) if shards else 1.0
    drawn = jax.random.normal(own_key, extent, jnp.float32) * width * gain
    return jnp.minimum(jnp.maximum(drawn, -reach), reach).astype(kind)


def setup_inputs(seed: int = 0) -> dict:
    arg_keys = jax.random.split(jax.random.key(seed), 20)
    return {
        "tokens": gaussian(arg_keys[0], (REQS, NEW, D), 1.0, 6.0, ((0, 4),)),
        "lengths": ragged(arg_keys[1], REQS, REQS * SEQ * 2 // 5, SEQ, 2).astype(jnp.int32),
        "slot_request": jax.random.permutation(arg_keys[2], REQS).astype(jnp.int32),
        "ln1_gain": jnp.clip(1.0 + 0.1 * jax.random.normal(arg_keys[3], (D,), jnp.float32), 0.5, 1.5),
        "ln1_bias": gaussian(arg_keys[4], (D,), 0.5, 3.0, (), jnp.float32),
        "w_query": gaussian(arg_keys[5], (D, D), D ** -0.5, 0.125, ((1, 64),)),
        "w_key": gaussian(arg_keys[6], (D, D), D ** -0.5, 0.125, ((1, 64),)),
        "w_value": gaussian(arg_keys[7], (D, D), D ** -0.5, 0.125, ((1, 64),)),
        "b_query": draw_b_query(jax.random.fold_in(arg_keys[19], 71), 0),
        "b_key": draw_b_key(jax.random.fold_in(arg_keys[19], 71), 0),
        "b_value": gaussian(arg_keys[10], (D,), 0.5, 3.0, ((0, 64),), jnp.float32),
        "cache_keys": draw_cache_keys(jax.random.fold_in(arg_keys[19], 71), 0),
        "cache_values": gaussian(arg_keys[12], (REQS, SEQ, D), 1.5, 9.0, ((0, 4), (1, 64))),
        "w_out": gaussian(arg_keys[13], (D, D), D ** -0.5, 0.125, ((1, 64),)),
        "ln2_gain": jnp.clip(1.0 + 0.1 * jax.random.normal(arg_keys[14], (D,), jnp.float32), 0.5, 1.5),
        "ln2_bias": gaussian(arg_keys[15], (D,), 0.5, 3.0, (), jnp.float32),
        "w_gate": gaussian(arg_keys[16], (D, FF), D ** -0.5, 0.125, ((1, 64),)),
        "w_up": gaussian(arg_keys[17], (D, FF), D ** -0.5, 0.125, ((1, 64),)),
        "w_down": gaussian(arg_keys[18], (FF, D), FF ** -0.5, 0.078125, ((0, 64),)),
    }


def layer_norm(values, norm_gain, norm_bias):
    average = lax.optimization_barrier(jnp.mean(values, -1, keepdims=True))
    centered = values - average
    variance = lax.optimization_barrier(jnp.mean(centered * centered, -1, keepdims=True))
    return centered * lax.rsqrt(variance + 1e-05) * norm_gain + norm_bias

def rotate(heads, positions):
    half_rot = ROT // 2
    frequency = 10000.0 ** (-2.0 * jnp.arange(half_rot, dtype=jnp.float32) / ROT)
    angles = positions.astype(jnp.float32)[..., None, None] * frequency
    cosine = jnp.cos(angles)
    sine = jnp.sin(angles)
    leading = heads[..., :half_rot]
    second = heads[..., half_rot:ROT]
    unrotated = heads[..., ROT:]
    return jnp.concatenate([leading * cosine - second * sine, second * cosine + leading * sine, unrotated], -1)

def reference(tokens, lengths, slot_request, ln1_gain, ln1_bias, w_query, w_key, w_value, b_query, b_key, b_value, cache_keys, cache_values, w_out, ln2_gain, ln2_bias, w_gate, w_up, w_down):
    inputs = jnp.take(tokens, slot_request, axis=0).astype(jnp.float32)
    spans = jnp.take(lengths, slot_request)
    token_rows = inputs.reshape(REQS * NEW, D)
    normed = layer_norm(token_rows, ln1_gain, ln1_bias).astype(jnp.bfloat16)
    query_raw = (jnp.dot(normed, w_query, preferred_element_type=jnp.float32) + b_query).astype(jnp.bfloat16)
    key_raw = (jnp.dot(normed, w_key, preferred_element_type=jnp.float32) + b_key).astype(jnp.bfloat16)
    value_raw = (jnp.dot(normed, w_value, preferred_element_type=jnp.float32) + b_value).astype(jnp.bfloat16)
    positions = spans[:, None] + jnp.arange(NEW, dtype=jnp.int32)[None, :]
    head_shape = (REQS, NEW, HEADS, HEAD_DIM)
    queries = rotate(query_raw.astype(jnp.float32).reshape(head_shape), positions).astype(jnp.bfloat16)
    keys_new = rotate(key_raw.astype(jnp.float32).reshape(head_shape), positions).astype(jnp.bfloat16)
    values_new = value_raw.reshape(head_shape)
    score_scale = HEAD_DIM ** (-0.5)

    def attend_one(packed):
        query_one, key_one, value_one, cache_key_one, cache_value_one, length = packed
        query_float = query_one.astype(jnp.float32)
        key_blocks = cache_key_one.reshape(N_BLK, BLK_LEN, HEADS, HEAD_DIM).astype(jnp.float32)
        value_blocks = cache_value_one.reshape(N_BLK, BLK_LEN, HEADS, HEAD_DIM).astype(jnp.float32)
        scores = jnp.einsum('thd,bphd->bthp', query_float, key_blocks) * score_scale
        places = jnp.arange(N_BLK * BLK_LEN, dtype=jnp.int32).reshape(N_BLK, 1, 1, BLK_LEN)
        visible = places < length
        block_peak = lax.optimization_barrier(jnp.max(jnp.where(visible, scores, -1e+30), -1))
        weights = jnp.where(visible, jnp.exp(scores - block_peak[..., None]), 0.0)
        block_total = lax.optimization_barrier(jnp.sum(weights, -1))
        rounded = lax.optimization_barrier(weights.astype(jnp.bfloat16)).astype(jnp.float32)
        block_sum = jnp.einsum('bthp,bphd->bthd', rounded, value_blocks)
        fresh_scores = jnp.einsum('thd,shd->ths', query_float, key_one.astype(jnp.float32)) * score_scale
        causal = jnp.arange(NEW)[:, None, None] >= jnp.arange(NEW)[None, None, :]
        fresh_peak = lax.optimization_barrier(jnp.max(jnp.where(causal, fresh_scores, -1e+30), -1))
        fresh_weights = jnp.where(causal, jnp.exp(fresh_scores - fresh_peak[..., None]), 0.0)
        fresh_total = lax.optimization_barrier(jnp.sum(fresh_weights, -1))
        fresh_rounded = lax.optimization_barrier(fresh_weights.astype(jnp.bfloat16)).astype(jnp.float32)
        fresh_sum = jnp.einsum('ths,shd->thd', fresh_rounded, value_one.astype(jnp.float32))
        peak_all = jnp.maximum(lax.optimization_barrier(jnp.max(block_peak, 0)), fresh_peak)
        scale_old = jnp.exp(block_peak - peak_all)
        scale_new = jnp.exp(fresh_peak - peak_all)
        total_all = lax.optimization_barrier(jnp.sum(block_total * scale_old, 0)) + fresh_total * scale_new
        accum_all = lax.optimization_barrier(jnp.sum(block_sum * scale_old[..., None], 0)) + fresh_sum * scale_new[..., None]
        return (accum_all / total_all[..., None]).astype(jnp.bfloat16)
    attended = lax.map(attend_one, (queries, keys_new, values_new, cache_keys, cache_values, spans))
    residual = token_rows + jnp.dot(attended.reshape(REQS * NEW, D), w_out, preferred_element_type=jnp.float32)
    normed_two = layer_norm(residual, ln2_gain, ln2_bias).astype(jnp.bfloat16)
    gate_proj = jnp.dot(normed_two, w_gate, preferred_element_type=jnp.float32)
    up_proj = jnp.dot(normed_two, w_up, preferred_element_type=jnp.float32)
    hidden = (jax.nn.silu(gate_proj) * up_proj).astype(jnp.bfloat16)
    layer_rows = residual + jnp.dot(hidden, w_down, preferred_element_type=jnp.float32)
    layer_out = layer_rows.astype(jnp.bfloat16).reshape(REQS, NEW, D)
    return (layer_out, keys_new.reshape(REQS, NEW, D), values_new.reshape(REQS, NEW, D))
```

```python
import jax
import jax.numpy as jnp
from jax import lax
from jax.sharding import PartitionSpec as P

D = 2048
HEADS = 32
HEAD_DIM = 64
ROT = 16
NEW = 4


def layer_norm(values, norm_gain, norm_bias):
    average = jnp.mean(values, -1, keepdims=True)
    centered = values - average
    variance = jnp.mean(centered * centered, -1, keepdims=True)
    return centered * lax.rsqrt(variance + 1e-05) * norm_gain + norm_bias


def rotate(heads, positions):
    half_rot = ROT // 2
    frequency = 10000.0 ** (-2.0 * jnp.arange(half_rot, dtype=jnp.float32) / ROT)
    angles = positions.astype(jnp.float32)[..., None, None] * frequency
    cosine = jnp.cos(angles)
    sine = jnp.sin(angles)
    leading = heads[..., :half_rot]
    second = heads[..., half_rot:ROT]
    unrotated = heads[..., ROT:]
    return jnp.concatenate(
        [leading * cosine - second * sine, second * cosine + leading * sine, unrotated], -1
    )


def xor_pairs(count, bit):
    return [(i, i ^ (1 << bit)) for i in range(count)]


def bit_of(index, bit):
    return (index // (1 << bit)) % 2


def gather_blk(part, count, order):
    index = lax.axis_index("blk")
    bits = count.bit_length() - 1
    buffer = part
    done = []
    for bit in order:
        other = lax.ppermute(buffer, "blk", xor_pairs(count, bit))
        low = bit_of(index, bit) == 0
        buffer = jnp.where(low, jnp.stack([buffer, other]), jnp.stack([other, buffer]))
        done.insert(0, bit)
    axes = [done.index(bit) for bit in range(bits - 1, -1, -1)]
    axes += list(range(bits, bits + part.ndim))
    return buffer.transpose(axes).reshape((count,) + part.shape)


def scatter_sum_blk(chunks, count, order):
    index = lax.axis_index("blk")
    bits = count.bit_length() - 1
    buffer = chunks.reshape((2,) * bits + chunks.shape[1:])
    remaining = list(range(bits - 1, -1, -1))
    for bit in order:
        axis = remaining.index(bit)
        low = bit_of(index, bit) == 0
        first = lax.index_in_dim(buffer, 0, axis, keepdims=False)
        second = lax.index_in_dim(buffer, 1, axis, keepdims=False)
        keep = jnp.where(low, first, second)
        send = jnp.where(low, second, first)
        buffer = keep + lax.ppermute(send, "blk", xor_pairs(count, bit))
        remaining.pop(axis)
    return buffer


def merge_blocks(peak, total, accum, count):
    bits = count.bit_length() - 1
    for bit in range(bits):
        pairs = xor_pairs(count, bit)
        peak_other = lax.ppermute(peak, "blk", pairs)
        total_other = lax.ppermute(total, "blk", pairs)
        accum_other = lax.ppermute(accum, "blk", pairs)
        peak_new = jnp.maximum(peak, peak_other)
        scale_own = jnp.exp(peak - peak_new)
        scale_other = jnp.exp(peak_other - peak_new)
        total = total * scale_own + total_other * scale_other
        accum = accum * scale_own[..., None] + accum_other * scale_other[..., None]
        peak = peak_new
    return peak, total, accum


def body(
    tokens,
    lengths,
    slot_request,
    ln1_gain,
    ln1_bias,
    w_query,
    w_key,
    w_value,
    b_query,
    b_key,
    b_value,
    cache_keys,
    cache_values,
    w_out,
    ln2_gain,
    ln2_bias,
    w_gate,
    w_up,
    w_down,
):
    group_index = lax.axis_index("req")
    block_index = lax.axis_index("blk")
    count_req = tokens.shape[0]
    block_len = cache_keys.shape[1]
    col_count = w_query.shape[1]
    row_total = count_req * NEW
    column_start = block_index * col_count
    gathered = lax.all_gather(tokens, "req", axis=0, tiled=True)
    owned_slots = lax.dynamic_slice_in_dim(slot_request, group_index * count_req, count_req)
    inputs = jnp.take(gathered, owned_slots, axis=0).astype(jnp.float32)
    span_lengths = jnp.take(lengths, owned_slots)
    token_rows = inputs.reshape(row_total, D)
    normed = layer_norm(token_rows, ln1_gain, ln1_bias).astype(jnp.bfloat16)
    query_cols = (jnp.dot(normed, w_query, preferred_element_type=jnp.float32) + b_query).astype(
        jnp.bfloat16
    )
    key_cols = (jnp.dot(normed, w_key, preferred_element_type=jnp.float32) + b_key).astype(
        jnp.bfloat16
    )
    value_cols = (jnp.dot(normed, w_value, preferred_element_type=jnp.float32) + b_value).astype(
        jnp.bfloat16
    )
    count_blk = D // col_count
    packed = jnp.concatenate([query_cols, key_cols, value_cols], 1)
    gathered_cols = gather_blk(packed, count_blk, tuple(range(count_blk.bit_length() - 2, -1, -1)))
    whole_cols = gathered_cols.transpose(1, 0, 2)
    query_raw = whole_cols[:, :, :col_count].reshape(row_total, D)
    key_raw = whole_cols[:, :, col_count : 2 * col_count].reshape(row_total, D)
    value_raw = whole_cols[:, :, 2 * col_count :].reshape(row_total, D)
    positions = span_lengths[:, None] + jnp.arange(NEW, dtype=jnp.int32)[None, :]
    head_shape = (count_req, NEW, HEADS, HEAD_DIM)
    queries = rotate(query_raw.astype(jnp.float32).reshape(head_shape), positions).astype(
        jnp.bfloat16
    )
    keys_new = rotate(key_raw.astype(jnp.float32).reshape(head_shape), positions).astype(
        jnp.bfloat16
    )
    values_new = value_raw.reshape(head_shape)
    new_keys_out = lax.dynamic_slice_in_dim(
        keys_new.reshape(count_req, NEW, D), column_start, col_count, 2
    )
    new_values_out = lax.dynamic_slice_in_dim(
        value_raw.reshape(count_req, NEW, D), column_start, col_count, 2
    )
    score_scale = HEAD_DIM ** (-0.5)
    key_heads = cache_keys.reshape(count_req, block_len, HEADS, HEAD_DIM)
    value_heads = cache_values.reshape(count_req, block_len, HEADS, HEAD_DIM)
    scores = (
        jnp.einsum("rthd,rphd->rthp", queries, key_heads, preferred_element_type=jnp.float32)
        * score_scale
    )
    places = block_index * block_len + jnp.arange(block_len, dtype=jnp.int32)
    visible = places[None, None, None, :] < span_lengths[:, None, None, None]
    peak_local = jnp.max(jnp.where(visible, scores, -1e30), -1)
    weights = jnp.where(visible, jnp.exp(scores - peak_local[..., None]), 0.0)
    total_local = jnp.sum(weights, -1)
    accum_local = jnp.einsum(
        "rthp,rphd->rthd",
        weights.astype(jnp.bfloat16),
        value_heads,
        preferred_element_type=jnp.float32,
    )
    fresh_scores = (
        jnp.einsum("rthd,rshd->rths", queries, keys_new, preferred_element_type=jnp.float32)
        * score_scale
    )
    causal = jnp.arange(NEW)[:, None, None] >= jnp.arange(NEW)[None, None, :]
    fresh_peak = jnp.max(jnp.where(causal, fresh_scores, -1e30), -1)
    fresh_weights = jnp.where(causal, jnp.exp(fresh_scores - fresh_peak[..., None]), 0.0)
    fresh_total = jnp.sum(fresh_weights, -1)
    fresh_accum = jnp.einsum(
        "rths,rshd->rthd",
        fresh_weights.astype(jnp.bfloat16),
        values_new,
        preferred_element_type=jnp.float32,
    )
    cache_peak, cache_total, cache_accum = merge_blocks(
        peak_local, total_local, accum_local, count_blk
    )
    peak_all = jnp.maximum(cache_peak, fresh_peak)
    scale_cache = jnp.exp(cache_peak - peak_all)
    scale_new = jnp.exp(fresh_peak - peak_all)
    numer = cache_accum * scale_cache[..., None] + fresh_accum * scale_new[..., None]
    denom = cache_total * scale_cache + fresh_total * scale_new
    attended = (numer / denom[..., None]).astype(jnp.bfloat16).reshape(row_total, D)
    input_cols = lax.dynamic_slice_in_dim(token_rows, column_start, col_count, 1)
    residual = input_cols + jnp.dot(attended, w_out, preferred_element_type=jnp.float32)
    gathered_rows = gather_blk(residual, count_blk, tuple(range(count_blk.bit_length() - 2, -1, -1)))
    whole_rows = gathered_rows.transpose(1, 0, 2).reshape(row_total, D)
    normed_two = layer_norm(whole_rows, ln2_gain, ln2_bias).astype(jnp.bfloat16)
    gate_proj = jnp.dot(normed_two, w_gate, preferred_element_type=jnp.float32)
    up_proj = jnp.dot(normed_two, w_up, preferred_element_type=jnp.float32)
    hidden = (jax.nn.silu(gate_proj) * up_proj).astype(jnp.bfloat16)
    down_part = jnp.dot(hidden, w_down, preferred_element_type=jnp.float32)
    down_chunks = down_part.reshape(row_total, count_blk, col_count).transpose(1, 0, 2)
    down_cols = scatter_sum_blk(down_chunks, count_blk, tuple(range(count_blk.bit_length() - 1)))
    layer_rows = (residual + down_cols).astype(jnp.bfloat16)
    return (layer_rows.reshape(count_req, NEW, col_count), new_keys_out, new_values_out)


def solution(mesh):
    return jax.shard_map(
        body,
        mesh=mesh,
        in_specs=(
            P("req", None, None),
            P(),
            P(),
            P(),
            P(),
            P(None, "blk"),
            P(None, "blk"),
            P(None, "blk"),
            P("blk"),
            P("blk"),
            P("blk"),
            P("req", "blk", None),
            P("req", "blk", None),
            P(None, "blk"),
            P(),
            P(),
            P(None, "blk"),
            P(None, "blk"),
            P("blk", None),
        ),
        out_specs=(P("req", None, "blk"), P("req", None, "blk"), P("req", None, "blk")),
        check_vma=False,
    )
```

```python
import jax
import jax.numpy as jnp
from jax import lax
from jax.sharding import PartitionSpec as P

D = 2048
HEADS = 32
HEAD_DIM = 64
ROT = 16
NEW = 4


def layer_norm(values, norm_gain, norm_bias):
    average = jnp.mean(values, -1, keepdims=True)
    centered = values - average
    variance = jnp.mean(centered * centered, -1, keepdims=True)
    return centered * lax.rsqrt(variance + 1e-05) * norm_gain + norm_bias


def rotate(heads, positions):
    half_rot = ROT // 2
    frequency = 10000.0 ** (-2.0 * jnp.arange(half_rot, dtype=jnp.float32) / ROT)
    angles = positions.astype(jnp.float32)[..., None, None] * frequency
    cosine = jnp.cos(angles)
    sine = jnp.sin(angles)
    leading = heads[..., :half_rot]
    second = heads[..., half_rot:ROT]
    unrotated = heads[..., ROT:]
    return jnp.concatenate(
        [leading * cosine - second * sine, second * cosine + leading * sine, unrotated], -1
    )


def xor_pairs(count, bit):
    return [(i, i ^ (1 << bit)) for i in range(count)]


def bit_of(index, bit):
    return (index // (1 << bit)) % 2


def gather_blk(part, count, order, axis_name="blk"):
    index = lax.axis_index(axis_name)
    bits = count.bit_length() - 1
    buffer = part
    done = []
    for bit in order:
        other = lax.ppermute(buffer, axis_name, xor_pairs(count, bit))
        low = bit_of(index, bit) == 0
        buffer = jnp.where(low, jnp.stack([buffer, other]), jnp.stack([other, buffer]))
        done.insert(0, bit)
    axes = [done.index(bit) for bit in range(bits - 1, -1, -1)]
    axes += list(range(bits, bits + part.ndim))
    return buffer.transpose(axes).reshape((count,) + part.shape)


def scatter_sum_blk(chunks, count, order):
    index = lax.axis_index("blk")
    bits = count.bit_length() - 1
    buffer = chunks.reshape((2,) * bits + chunks.shape[1:])
    remaining = list(range(bits - 1, -1, -1))
    for bit in order:
        axis = remaining.index(bit)
        low = bit_of(index, bit) == 0
        first = lax.index_in_dim(buffer, 0, axis, keepdims=False)
        second = lax.index_in_dim(buffer, 1, axis, keepdims=False)
        keep = jnp.where(low, first, second)
        send = jnp.where(low, second, first)
        buffer = keep + lax.ppermute(send, "blk", xor_pairs(count, bit))
        remaining.pop(axis)
    return buffer


def merge_rows(own, other):
    width = own.shape[-1] - 2
    peak_own, peak_other = own[..., width], other[..., width]
    peak = jnp.maximum(peak_own, peak_other)
    scale_own = jnp.exp(peak_own - peak)[..., None]
    scale_other = jnp.exp(peak_other - peak)[..., None]
    sums = own[..., :width] * scale_own + other[..., :width] * scale_other
    total = own[..., width + 1 :] * scale_own + other[..., width + 1 :] * scale_other
    return jnp.concatenate([sums, peak[..., None], total], -1)


def scatter_merge_blk(chunks, count, order):
    index = lax.axis_index("blk")
    bits = count.bit_length() - 1
    buffer = chunks.reshape((2,) * bits + chunks.shape[1:])
    remaining = list(range(bits - 1, -1, -1))
    for bit in order:
        axis = remaining.index(bit)
        low = bit_of(index, bit) == 0
        first = lax.index_in_dim(buffer, 0, axis, keepdims=False)
        second = lax.index_in_dim(buffer, 1, axis, keepdims=False)
        keep = jnp.where(low, first, second)
        send = jnp.where(low, second, first)
        buffer = merge_rows(keep, lax.ppermute(send, "blk", xor_pairs(count, bit)))
        remaining.pop(axis)
    return buffer


def body(
    tokens,
    lengths,
    slot_request,
    ln1_gain,
    ln1_bias,
    w_query,
    w_key,
    w_value,
    b_query,
    b_key,
    b_value,
    cache_keys,
    cache_values,
    w_out,
    ln2_gain,
    ln2_bias,
    w_gate,
    w_up,
    w_down,
):
    group_index = lax.axis_index("req")
    block_index = lax.axis_index("blk")
    count_req = tokens.shape[0]
    block_len = cache_keys.shape[1]
    col_count = w_query.shape[1]
    row_total = count_req * NEW
    column_start = block_index * col_count
    count_group = slot_request.shape[0] // count_req
    gathered = gather_blk(
        tokens, count_group, tuple(range(count_group.bit_length() - 1)), "req"
    ).reshape((count_group * count_req,) + tokens.shape[1:])
    owned_slots = lax.dynamic_slice_in_dim(slot_request, group_index * count_req, count_req)
    inputs = jnp.take(gathered, owned_slots, axis=0).astype(jnp.float32)
    span_lengths = jnp.take(lengths, owned_slots)
    token_rows = inputs.reshape(row_total, D)
    normed = layer_norm(token_rows, ln1_gain, ln1_bias).astype(jnp.bfloat16)
    query_cols = (jnp.dot(normed, w_query, preferred_element_type=jnp.float32) + b_query).astype(
        jnp.bfloat16
    )
    key_cols = (jnp.dot(normed, w_key, preferred_element_type=jnp.float32) + b_key).astype(
        jnp.bfloat16
    )
    value_cols = (jnp.dot(normed, w_value, preferred_element_type=jnp.float32) + b_value).astype(
        jnp.bfloat16
    )
    count_blk = D // col_count
    packed = jnp.concatenate([query_cols, key_cols, value_cols], 1)
    gathered_cols = gather_blk(packed, count_blk, tuple(range(count_blk.bit_length() - 2, -1, -1)))
    whole_cols = gathered_cols.transpose(1, 0, 2)
    query_raw = whole_cols[:, :, :col_count].reshape(row_total, D)
    key_raw = whole_cols[:, :, col_count : 2 * col_count].reshape(row_total, D)
    value_raw = whole_cols[:, :, 2 * col_count :].reshape(row_total, D)
    positions = span_lengths[:, None] + jnp.arange(NEW, dtype=jnp.int32)[None, :]
    head_shape = (count_req, NEW, HEADS, HEAD_DIM)
    queries = rotate(query_raw.astype(jnp.float32).reshape(head_shape), positions).astype(
        jnp.bfloat16
    )
    keys_new = rotate(key_raw.astype(jnp.float32).reshape(head_shape), positions).astype(
        jnp.bfloat16
    )
    values_new = value_raw.reshape(head_shape)
    new_keys_out = lax.dynamic_slice_in_dim(
        keys_new.reshape(count_req, NEW, D), column_start, col_count, 2
    )
    new_values_out = lax.dynamic_slice_in_dim(
        value_raw.reshape(count_req, NEW, D), column_start, col_count, 2
    )
    score_scale = HEAD_DIM ** (-0.5)
    key_heads = cache_keys.reshape(count_req, block_len, HEADS, HEAD_DIM)
    value_heads = cache_values.reshape(count_req, block_len, HEADS, HEAD_DIM)
    scores = (
        jnp.einsum("rthd,rphd->rthp", queries, key_heads, preferred_element_type=jnp.float32)
        * score_scale
    )
    places = block_index * block_len + jnp.arange(block_len, dtype=jnp.int32)
    visible = places[None, None, None, :] < span_lengths[:, None, None, None]
    peak_local = jnp.max(jnp.where(visible, scores, -1e30), -1)
    weights = jnp.where(visible, jnp.exp(scores - peak_local[..., None]), 0.0)
    total_local = jnp.sum(weights, -1)
    accum_local = jnp.einsum(
        "rthp,rphd->rthd",
        weights.astype(jnp.bfloat16),
        value_heads,
        preferred_element_type=jnp.float32,
    )
    fresh_scores = (
        jnp.einsum("rthd,rshd->rths", queries, keys_new, preferred_element_type=jnp.float32)
        * score_scale
    )
    causal = jnp.arange(NEW)[:, None, None] >= jnp.arange(NEW)[None, None, :]
    fresh_peak = jnp.max(jnp.where(causal, fresh_scores, -1e30), -1)
    fresh_weights = jnp.where(causal, jnp.exp(fresh_scores - fresh_peak[..., None]), 0.0)
    fresh_total = jnp.sum(fresh_weights, -1)
    fresh_accum = jnp.einsum(
        "rths,rshd->rthd",
        fresh_weights.astype(jnp.bfloat16),
        values_new,
        preferred_element_type=jnp.float32,
    )
    head_rows = row_total * HEADS
    share = head_rows // count_blk
    packed_rows = jnp.concatenate(
        [
            accum_local.reshape(head_rows, HEAD_DIM),
            peak_local.reshape(head_rows, 1),
            total_local.reshape(head_rows, 1),
        ],
        -1,
    ).reshape(count_blk, share, HEAD_DIM + 2)
    merged = scatter_merge_blk(packed_rows, count_blk, tuple(range(count_blk.bit_length() - 1)))
    cache_accum = merged[:, :HEAD_DIM]
    cache_peak = merged[:, HEAD_DIM]
    cache_total = merged[:, HEAD_DIM + 1]
    row_start = block_index * share
    fresh_peak_own = lax.dynamic_slice_in_dim(fresh_peak.reshape(head_rows), row_start, share)
    fresh_total_own = lax.dynamic_slice_in_dim(fresh_total.reshape(head_rows), row_start, share)
    fresh_accum_own = lax.dynamic_slice_in_dim(
        fresh_accum.reshape(head_rows, HEAD_DIM), row_start, share
    )
    peak_all = jnp.maximum(cache_peak, fresh_peak_own)
    scale_cache = jnp.exp(cache_peak - peak_all)
    scale_new = jnp.exp(fresh_peak_own - peak_all)
    numer = cache_accum * scale_cache[:, None] + fresh_accum_own * scale_new[:, None]
    denom = cache_total * scale_cache + fresh_total_own * scale_new
    attended_own = (numer / denom[:, None]).astype(jnp.bfloat16)
    attended = gather_blk(
        attended_own, count_blk, tuple(range(count_blk.bit_length() - 2, -1, -1))
    ).reshape(row_total, D)
    input_cols = lax.dynamic_slice_in_dim(token_rows, column_start, col_count, 1)
    residual = input_cols + jnp.dot(attended, w_out, preferred_element_type=jnp.float32)
    gathered_rows = gather_blk(residual, count_blk, tuple(range(count_blk.bit_length() - 2, -1, -1)))
    whole_rows = gathered_rows.transpose(1, 0, 2).reshape(row_total, D)
    normed_two = layer_norm(whole_rows, ln2_gain, ln2_bias).astype(jnp.bfloat16)
    gate_proj = jnp.dot(normed_two, w_gate, preferred_element_type=jnp.float32)
    up_proj = jnp.dot(normed_two, w_up, preferred_element_type=jnp.float32)
    hidden = (jax.nn.silu(gate_proj) * up_proj).astype(jnp.bfloat16)
    down_part = jnp.dot(hidden, w_down, preferred_element_type=jnp.float32)
    down_chunks = down_part.reshape(row_total, count_blk, col_count).transpose(1, 0, 2)
    down_cols = scatter_sum_blk(down_chunks, count_blk, tuple(range(count_blk.bit_length() - 1)))
    layer_rows = (residual + down_cols).astype(jnp.bfloat16)
    return (layer_rows.reshape(count_req, NEW, col_count), new_keys_out, new_values_out)


def solution(mesh):
    return jax.shard_map(
        body,
        mesh=mesh,
        in_specs=(
            P("req", None, None),
            P(),
            P(),
            P(),
            P(),
            P(None, "blk"),
            P(None, "blk"),
            P(None, "blk"),
            P("blk"),
            P("blk"),
            P("blk"),
            P("req", "blk", None),
            P("req", "blk", None),
            P(None, "blk"),
            P(),
            P(),
            P(None, "blk"),
            P(None, "blk"),
            P("blk", None),
        ),
        out_specs=(P("req", None, "blk"), P("req", None, "blk"), P("req", None, "blk")),
        check_vma=False,
    )
```

```python
import jax
import jax.numpy as jnp
from jax import lax
from jax.sharding import PartitionSpec as P

D = 2048
HEADS = 32
HEAD_DIM = 64
ROT = 16
NEW = 4


def layer_norm(values, norm_gain, norm_bias):
    average = jnp.mean(values, -1, keepdims=True)
    centered = values - average
    variance = jnp.mean(centered * centered, -1, keepdims=True)
    return centered * lax.rsqrt(variance + 1e-05) * norm_gain + norm_bias


def rotate(heads, positions):
    half_rot = ROT // 2
    frequency = 10000.0 ** (-2.0 * jnp.arange(half_rot, dtype=jnp.float32) / ROT)
    angles = positions.astype(jnp.float32)[..., None, None] * frequency
    cosine = jnp.cos(angles)
    sine = jnp.sin(angles)
    leading = heads[..., :half_rot]
    second = heads[..., half_rot:ROT]
    unrotated = heads[..., ROT:]
    return jnp.concatenate(
        [leading * cosine - second * sine, second * cosine + leading * sine, unrotated], -1
    )


BLK_GROUPS_UP = ((0, 1), (2, 3), (4, 5))
BLK_GROUPS_DOWN = ((4, 5), (2, 3), (0, 1))


def bit_of(index, bit):
    return (index // (1 << bit)) % 2


def group_digit(index, bits):
    return sum(bit_of(index, bit) * (1 << place) for place, bit in enumerate(bits))


def group_offset(step, bits):
    return sum(((step >> place) & 1) << bit for place, bit in enumerate(bits))


def exchange(value, axis_name, count, offset):
    return lax.ppermute(value, axis_name, [(i, i ^ offset) for i in range(count)])


def fit_groups(groups, count):
    bits = count.bit_length() - 1
    kept = tuple(tuple(b for b in group if b < bits) for group in groups)
    kept = tuple(group for group in kept if group)
    covered = sorted(b for group in kept for b in group)
    if covered != list(range(bits)):
        kept = tuple((b,) for b in range(bits))
    return kept


def gather_axis(part, count, groups, axis_name="blk"):
    index = lax.axis_index(axis_name)
    bits = count.bit_length() - 1
    buffer = part
    labels = []
    for group in fit_groups(groups, count):
        size = 1 << len(group)
        digit = group_digit(index, group)
        received = [buffer]
        for step in range(1, size):
            received.append(exchange(buffer, axis_name, count, group_offset(step, group)))
        stacked = jnp.stack(received)
        buffer = jnp.take(stacked, jnp.arange(size, dtype=jnp.int32) ^ digit, axis=0)
        labels = list(reversed(group)) + labels
    buffer = buffer.reshape((2,) * bits + part.shape)
    axes = [labels.index(b) for b in range(bits - 1, -1, -1)]
    axes += list(range(bits, bits + part.ndim))
    return buffer.transpose(axes).reshape((count,) + part.shape)


def sum_parts(parts):
    result = parts[0]
    for part in parts[1:]:
        result = result + part
    return result


def merge_parts(parts):
    width = parts[0].shape[-1] - 2
    peak = parts[0][..., width]
    for part in parts[1:]:
        peak = jnp.maximum(peak, part[..., width])
    merged = None
    for part in parts:
        scaled = part[..., :width] * jnp.exp(part[..., width] - peak)[..., None]
        total = part[..., width + 1 :] * jnp.exp(part[..., width] - peak)[..., None]
        both = jnp.concatenate([scaled, total], -1)
        merged = both if merged is None else merged + both
    return jnp.concatenate([merged[..., :width], peak[..., None], merged[..., width:]], -1)


def scatter_axis(chunks, count, groups, combine, axis_name="blk"):
    index = lax.axis_index(axis_name)
    bits = count.bit_length() - 1
    rest = chunks.shape[1:]
    buffer = chunks.reshape((2,) * bits + rest)
    labels = list(range(bits - 1, -1, -1))
    for group in fit_groups(groups, count):
        size = 1 << len(group)
        lead = [labels.index(b) for b in reversed(group)]
        others = [axis for axis in range(len(labels)) if axis not in lead]
        buffer = buffer.transpose(lead + others + list(range(len(labels), buffer.ndim)))
        labels = [labels[axis] for axis in others]
        buffer = buffer.reshape((size,) + buffer.shape[len(group) :])
        digit = group_digit(index, group)
        parts = [lax.dynamic_index_in_dim(buffer, digit, 0, keepdims=False)]
        for step in range(1, size):
            send = lax.dynamic_index_in_dim(buffer, digit ^ step, 0, keepdims=False)
            parts.append(exchange(send, axis_name, count, group_offset(step, group)))
        buffer = combine(parts)
    return buffer.reshape(rest)


def body(
    tokens,
    lengths,
    slot_request,
    ln1_gain,
    ln1_bias,
    w_query,
    w_key,
    w_value,
    b_query,
    b_key,
    b_value,
    cache_keys,
    cache_values,
    w_out,
    ln2_gain,
    ln2_bias,
    w_gate,
    w_up,
    w_down,
):
    group_index = lax.axis_index("req")
    block_index = lax.axis_index("blk")
    count_req = tokens.shape[0]
    block_len = cache_keys.shape[1]
    col_count = w_query.shape[1]
    row_total = count_req * NEW
    column_start = block_index * col_count
    count_group = slot_request.shape[0] // count_req
    gathered = gather_axis(
        tokens, count_group, (tuple(range(count_group.bit_length() - 1)),), "req"
    ).reshape((count_group * count_req,) + tokens.shape[1:])
    owned_slots = lax.dynamic_slice_in_dim(slot_request, group_index * count_req, count_req)
    inputs = jnp.take(gathered, owned_slots, axis=0).astype(jnp.float32)
    span_lengths = jnp.take(lengths, owned_slots)
    token_rows = inputs.reshape(row_total, D)
    normed = layer_norm(token_rows, ln1_gain, ln1_bias).astype(jnp.bfloat16)
    query_cols = (jnp.dot(normed, w_query, preferred_element_type=jnp.float32) + b_query).astype(
        jnp.bfloat16
    )
    key_cols = (jnp.dot(normed, w_key, preferred_element_type=jnp.float32) + b_key).astype(
        jnp.bfloat16
    )
    value_cols = (jnp.dot(normed, w_value, preferred_element_type=jnp.float32) + b_value).astype(
        jnp.bfloat16
    )
    count_blk = D // col_count
    packed = jnp.concatenate([query_cols, key_cols, value_cols], 1)
    gathered_cols = gather_axis(packed, count_blk, BLK_GROUPS_DOWN)
    whole_cols = gathered_cols.transpose(1, 0, 2)
    query_raw = whole_cols[:, :, :col_count].reshape(row_total, D)
    key_raw = whole_cols[:, :, col_count : 2 * col_count].reshape(row_total, D)
    value_raw = whole_cols[:, :, 2 * col_count :].reshape(row_total, D)
    positions = span_lengths[:, None] + jnp.arange(NEW, dtype=jnp.int32)[None, :]
    head_shape = (count_req, NEW, HEADS, HEAD_DIM)
    queries = rotate(query_raw.astype(jnp.float32).reshape(head_shape), positions).astype(
        jnp.bfloat16
    )
    keys_new = rotate(key_raw.astype(jnp.float32).reshape(head_shape), positions).astype(
        jnp.bfloat16
    )
    values_new = value_raw.reshape(head_shape)
    new_keys_out = lax.dynamic_slice_in_dim(
        keys_new.reshape(count_req, NEW, D), column_start, col_count, 2
    )
    new_values_out = lax.dynamic_slice_in_dim(
        value_raw.reshape(count_req, NEW, D), column_start, col_count, 2
    )
    score_scale = HEAD_DIM ** (-0.5)
    key_heads = cache_keys.reshape(count_req, block_len, HEADS, HEAD_DIM)
    value_heads = cache_values.reshape(count_req, block_len, HEADS, HEAD_DIM)
    scores = (
        jnp.einsum("rthd,rphd->rthp", queries, key_heads, preferred_element_type=jnp.float32)
        * score_scale
    )
    places = block_index * block_len + jnp.arange(block_len, dtype=jnp.int32)
    visible = places[None, None, None, :] < span_lengths[:, None, None, None]
    peak_local = jnp.max(jnp.where(visible, scores, -1e30), -1)
    weights = jnp.where(visible, jnp.exp(scores - peak_local[..., None]), 0.0)
    total_local = jnp.sum(weights, -1)
    accum_local = jnp.einsum(
        "rthp,rphd->rthd",
        weights.astype(jnp.bfloat16),
        value_heads,
        preferred_element_type=jnp.float32,
    )
    fresh_scores = (
        jnp.einsum("rthd,rshd->rths", queries, keys_new, preferred_element_type=jnp.float32)
        * score_scale
    )
    causal = jnp.arange(NEW)[:, None, None] >= jnp.arange(NEW)[None, None, :]
    fresh_peak = jnp.max(jnp.where(causal, fresh_scores, -1e30), -1)
    fresh_weights = jnp.where(causal, jnp.exp(fresh_scores - fresh_peak[..., None]), 0.0)
    fresh_total = jnp.sum(fresh_weights, -1)
    fresh_accum = jnp.einsum(
        "rths,rshd->rthd",
        fresh_weights.astype(jnp.bfloat16),
        values_new,
        preferred_element_type=jnp.float32,
    )
    head_rows = row_total * HEADS
    share = head_rows // count_blk
    packed_rows = jnp.concatenate(
        [
            accum_local.reshape(head_rows, HEAD_DIM),
            peak_local.reshape(head_rows, 1),
            total_local.reshape(head_rows, 1),
        ],
        -1,
    ).reshape(count_blk, share, HEAD_DIM + 2)
    merged = scatter_axis(packed_rows, count_blk, BLK_GROUPS_UP, merge_parts)
    cache_accum = merged[:, :HEAD_DIM]
    cache_peak = merged[:, HEAD_DIM]
    cache_total = merged[:, HEAD_DIM + 1]
    row_start = block_index * share
    fresh_peak_own = lax.dynamic_slice_in_dim(fresh_peak.reshape(head_rows), row_start, share)
    fresh_total_own = lax.dynamic_slice_in_dim(fresh_total.reshape(head_rows), row_start, share)
    fresh_accum_own = lax.dynamic_slice_in_dim(
        fresh_accum.reshape(head_rows, HEAD_DIM), row_start, share
    )
    peak_all = jnp.maximum(cache_peak, fresh_peak_own)
    scale_cache = jnp.exp(cache_peak - peak_all)
    scale_new = jnp.exp(fresh_peak_own - peak_all)
    numer = cache_accum * scale_cache[:, None] + fresh_accum_own * scale_new[:, None]
    denom = cache_total * scale_cache + fresh_total_own * scale_new
    attended_own = (numer / denom[:, None]).astype(jnp.bfloat16)
    attended = gather_axis(attended_own, count_blk, BLK_GROUPS_DOWN).reshape(row_total, D)
    input_cols = lax.dynamic_slice_in_dim(token_rows, column_start, col_count, 1)
    residual = input_cols + jnp.dot(attended, w_out, preferred_element_type=jnp.float32)
    gathered_rows = gather_axis(residual, count_blk, BLK_GROUPS_DOWN)
    whole_rows = gathered_rows.transpose(1, 0, 2).reshape(row_total, D)
    normed_two = layer_norm(whole_rows, ln2_gain, ln2_bias).astype(jnp.bfloat16)
    gate_proj = jnp.dot(normed_two, w_gate, preferred_element_type=jnp.float32)
    up_proj = jnp.dot(normed_two, w_up, preferred_element_type=jnp.float32)
    hidden = (jax.nn.silu(gate_proj) * up_proj).astype(jnp.bfloat16)
    down_part = jnp.dot(hidden, w_down, preferred_element_type=jnp.float32)
    down_chunks = down_part.reshape(row_total, count_blk, col_count).transpose(1, 0, 2)
    down_cols = scatter_axis(down_chunks, count_blk, BLK_GROUPS_UP, sum_parts)
    layer_rows = (residual + down_cols).astype(jnp.bfloat16)
    return (layer_rows.reshape(count_req, NEW, col_count), new_keys_out, new_values_out)


def solution(mesh):
    return jax.shard_map(
        body,
        mesh=mesh,
        in_specs=(
            P("req", None, None),
            P(),
            P(),
            P(),
            P(),
            P(None, "blk"),
            P(None, "blk"),
            P(None, "blk"),
            P("blk"),
            P("blk"),
            P("blk"),
            P("req", "blk", None),
            P("req", "blk", None),
            P(None, "blk"),
            P(),
            P(),
            P(None, "blk"),
            P(None, "blk"),
            P("blk", None),
        ),
        out_specs=(P("req", None, "blk"), P("req", None, "blk"), P("req", None, "blk")),
        check_vma=False,
    )
```

```python
import jax
import jax.numpy as jnp
from jax import lax
from jax.sharding import PartitionSpec as P

D = 2048
HEADS = 32
HEAD_DIM = 64
ROT = 16
NEW = 4


def layer_norm(values, norm_gain, norm_bias):
    average = jnp.mean(values, -1, keepdims=True)
    centered = values - average
    variance = jnp.mean(centered * centered, -1, keepdims=True)
    return centered * lax.rsqrt(variance + 1e-05) * norm_gain + norm_bias


def rotate(heads, positions):
    half_rot = ROT // 2
    frequency = 10000.0 ** (-2.0 * jnp.arange(half_rot, dtype=jnp.float32) / ROT)
    angles = positions.astype(jnp.float32)[..., None, None] * frequency
    cosine = jnp.cos(angles)
    sine = jnp.sin(angles)
    leading = heads[..., :half_rot]
    second = heads[..., half_rot:ROT]
    unrotated = heads[..., ROT:]
    return jnp.concatenate(
        [leading * cosine - second * sine, second * cosine + leading * sine, unrotated], -1
    )


BLK_GROUPS_UP = ((0, 1), (2, 3), (4, 5))
BLK_GROUPS_DOWN = ((4, 5), (2, 3), (0, 1))


def bit_of(index, bit):
    return (index // (1 << bit)) % 2


def group_digit(index, bits):
    return sum(bit_of(index, bit) * (1 << place) for place, bit in enumerate(bits))


def group_offset(step, bits):
    return sum(((step >> place) & 1) << bit for place, bit in enumerate(bits))


def exchange(value, axis_name, count, offset):
    return lax.ppermute(value, axis_name, [(i, i ^ offset) for i in range(count)])


def fit_groups(groups, count):
    bits = count.bit_length() - 1
    kept = tuple(tuple(b for b in group if b < bits) for group in groups)
    kept = tuple(group for group in kept if group)
    covered = sorted(b for group in kept for b in group)
    if covered != list(range(bits)):
        kept = tuple((b,) for b in range(bits))
    return kept


def gather_axis(part, count, groups, axis_name="blk"):
    index = lax.axis_index(axis_name)
    bits = count.bit_length() - 1
    buffer = part
    labels = []
    for group in fit_groups(groups, count):
        size = 1 << len(group)
        digit = group_digit(index, group)
        received = [buffer]
        for step in range(1, size):
            received.append(exchange(buffer, axis_name, count, group_offset(step, group)))
        stacked = jnp.stack(received)
        buffer = jnp.take(stacked, jnp.arange(size, dtype=jnp.int32) ^ digit, axis=0)
        labels = list(reversed(group)) + labels
    buffer = buffer.reshape((2,) * bits + part.shape)
    axes = [labels.index(b) for b in range(bits - 1, -1, -1)]
    axes += list(range(bits, bits + part.ndim))
    return buffer.transpose(axes).reshape((count,) + part.shape)


def sum_parts(parts):
    result = parts[0]
    for part in parts[1:]:
        result = result + part
    return result


def merge_parts(parts):
    width = parts[0].shape[-1] - 2
    peak = parts[0][..., width]
    for part in parts[1:]:
        peak = jnp.maximum(peak, part[..., width])
    merged = None
    for part in parts:
        scaled = part[..., :width] * jnp.exp(part[..., width] - peak)[..., None]
        total = part[..., width + 1 :] * jnp.exp(part[..., width] - peak)[..., None]
        both = jnp.concatenate([scaled, total], -1)
        merged = both if merged is None else merged + both
    return jnp.concatenate([merged[..., :width], peak[..., None], merged[..., width:]], -1)


def scatter_axis(chunks, count, groups, combine, axis_name="blk"):
    index = lax.axis_index(axis_name)
    bits = count.bit_length() - 1
    rest = chunks.shape[1:]
    buffer = chunks.reshape((2,) * bits + rest)
    labels = list(range(bits - 1, -1, -1))
    for group in fit_groups(groups, count):
        size = 1 << len(group)
        lead = [labels.index(b) for b in reversed(group)]
        others = [axis for axis in range(len(labels)) if axis not in lead]
        buffer = buffer.transpose(lead + others + list(range(len(labels), buffer.ndim)))
        labels = [labels[axis] for axis in others]
        buffer = buffer.reshape((size,) + buffer.shape[len(group) :])
        digit = group_digit(index, group)
        parts = [lax.dynamic_index_in_dim(buffer, digit, 0, keepdims=False)]
        for step in range(1, size):
            send = lax.dynamic_index_in_dim(buffer, digit ^ step, 0, keepdims=False)
            parts.append(exchange(send, axis_name, count, group_offset(step, group)))
        buffer = combine(parts)
    return buffer.reshape(rest)


def body(
    tokens,
    lengths,
    slot_request,
    ln1_gain,
    ln1_bias,
    w_query,
    w_key,
    w_value,
    b_query,
    b_key,
    b_value,
    cache_keys,
    cache_values,
    w_out,
    ln2_gain,
    ln2_bias,
    w_gate,
    w_up,
    w_down,
):
    group_index = lax.axis_index("req")
    block_index = lax.axis_index("blk")
    count_req = tokens.shape[0]
    block_len = cache_keys.shape[1]
    col_count = w_query.shape[1]
    row_total = count_req * NEW
    column_start = block_index * col_count
    count_group = slot_request.shape[0] // count_req
    gathered = gather_axis(
        tokens, count_group, (tuple(range(count_group.bit_length() - 1)),), "req"
    ).reshape((count_group * count_req,) + tokens.shape[1:])
    owned_slots = lax.dynamic_slice_in_dim(slot_request, group_index * count_req, count_req)
    keys_by_dim = jnp.swapaxes(cache_keys, 1, 2)
    values_by_dim = jnp.swapaxes(cache_values, 1, 2)
    gathered, keys_by_dim, values_by_dim = lax.optimization_barrier(
        (gathered, keys_by_dim, values_by_dim)
    )
    inputs = jnp.take(gathered, owned_slots, axis=0).astype(jnp.float32)
    span_lengths = jnp.take(lengths, owned_slots)
    token_rows = inputs.reshape(row_total, D)
    normed = layer_norm(token_rows, ln1_gain, ln1_bias).astype(jnp.bfloat16)
    query_cols = (jnp.dot(normed, w_query, preferred_element_type=jnp.float32) + b_query).astype(
        jnp.bfloat16
    )
    key_cols = (jnp.dot(normed, w_key, preferred_element_type=jnp.float32) + b_key).astype(
        jnp.bfloat16
    )
    value_cols = (jnp.dot(normed, w_value, preferred_element_type=jnp.float32) + b_value).astype(
        jnp.bfloat16
    )
    count_blk = D // col_count
    packed = jnp.concatenate([query_cols, key_cols, value_cols], 1)
    gathered_cols = gather_axis(packed, count_blk, BLK_GROUPS_DOWN)
    whole_cols = gathered_cols.transpose(1, 0, 2)
    query_raw = whole_cols[:, :, :col_count].reshape(row_total, D)
    key_raw = whole_cols[:, :, col_count : 2 * col_count].reshape(row_total, D)
    value_raw = whole_cols[:, :, 2 * col_count :].reshape(row_total, D)
    positions = span_lengths[:, None] + jnp.arange(NEW, dtype=jnp.int32)[None, :]
    head_shape = (count_req, NEW, HEADS, HEAD_DIM)
    queries = rotate(query_raw.astype(jnp.float32).reshape(head_shape), positions).astype(
        jnp.bfloat16
    )
    keys_new = rotate(key_raw.astype(jnp.float32).reshape(head_shape), positions).astype(
        jnp.bfloat16
    )
    values_new = value_raw.reshape(head_shape)
    new_keys_out = lax.dynamic_slice_in_dim(
        keys_new.reshape(count_req, NEW, D), column_start, col_count, 2
    )
    new_values_out = lax.dynamic_slice_in_dim(
        value_raw.reshape(count_req, NEW, D), column_start, col_count, 2
    )
    score_scale = HEAD_DIM ** (-0.5)
    key_heads = keys_by_dim.reshape(count_req, HEADS, HEAD_DIM, block_len)
    value_heads = values_by_dim.reshape(count_req, HEADS, HEAD_DIM, block_len)
    scores = (
        jnp.einsum("rthd,rhdp->rthp", queries, key_heads, preferred_element_type=jnp.float32)
        * score_scale
    )
    places = block_index * block_len + jnp.arange(block_len, dtype=jnp.int32)
    visible = places[None, None, None, :] < span_lengths[:, None, None, None]
    peak_local = jnp.max(jnp.where(visible, scores, -1e30), -1)
    weights = jnp.where(visible, jnp.exp(scores - peak_local[..., None]), 0.0)
    total_local = jnp.sum(weights, -1)
    accum_local = jnp.einsum(
        "rthp,rhdp->rthd",
        weights.astype(jnp.bfloat16),
        value_heads,
        preferred_element_type=jnp.float32,
    )
    fresh_scores = (
        jnp.einsum("rthd,rshd->rths", queries, keys_new, preferred_element_type=jnp.float32)
        * score_scale
    )
    causal = jnp.arange(NEW)[:, None, None] >= jnp.arange(NEW)[None, None, :]
    fresh_peak = jnp.max(jnp.where(causal, fresh_scores, -1e30), -1)
    fresh_weights = jnp.where(causal, jnp.exp(fresh_scores - fresh_peak[..., None]), 0.0)
    fresh_total = jnp.sum(fresh_weights, -1)
    fresh_accum = jnp.einsum(
        "rths,rshd->rthd",
        fresh_weights.astype(jnp.bfloat16),
        values_new,
        preferred_element_type=jnp.float32,
    )
    head_rows = row_total * HEADS
    share = head_rows // count_blk
    packed_rows = jnp.concatenate(
        [
            accum_local.reshape(head_rows, HEAD_DIM),
            peak_local.reshape(head_rows, 1),
            total_local.reshape(head_rows, 1),
        ],
        -1,
    ).reshape(count_blk, share, HEAD_DIM + 2)
    merged = scatter_axis(packed_rows, count_blk, BLK_GROUPS_UP, merge_parts)
    cache_accum = merged[:, :HEAD_DIM]
    cache_peak = merged[:, HEAD_DIM]
    cache_total = merged[:, HEAD_DIM + 1]
    row_start = block_index * share
    fresh_peak_own = lax.dynamic_slice_in_dim(fresh_peak.reshape(head_rows), row_start, share)
    fresh_total_own = lax.dynamic_slice_in_dim(fresh_total.reshape(head_rows), row_start, share)
    fresh_accum_own = lax.dynamic_slice_in_dim(
        fresh_accum.reshape(head_rows, HEAD_DIM), row_start, share
    )
    peak_all = jnp.maximum(cache_peak, fresh_peak_own)
    scale_cache = jnp.exp(cache_peak - peak_all)
    scale_new = jnp.exp(fresh_peak_own - peak_all)
    numer = cache_accum * scale_cache[:, None] + fresh_accum_own * scale_new[:, None]
    denom = cache_total * scale_cache + fresh_total_own * scale_new
    attended_own = (numer / denom[:, None]).astype(jnp.bfloat16)
    attended = gather_axis(attended_own, count_blk, BLK_GROUPS_DOWN).reshape(row_total, D)
    input_cols = lax.dynamic_slice_in_dim(token_rows, column_start, col_count, 1)
    residual = input_cols + jnp.dot(attended, w_out, preferred_element_type=jnp.float32)
    gathered_rows = gather_axis(residual.astype(jnp.bfloat16), count_blk, BLK_GROUPS_DOWN)
    whole_rows = gathered_rows.transpose(1, 0, 2).reshape(row_total, D).astype(jnp.float32)
    normed_two = layer_norm(whole_rows, ln2_gain, ln2_bias).astype(jnp.bfloat16)
    gate_proj = jnp.dot(normed_two, w_gate, preferred_element_type=jnp.float32)
    up_proj = jnp.dot(normed_two, w_up, preferred_element_type=jnp.float32)
    hidden = (jax.nn.silu(gate_proj) * up_proj).astype(jnp.bfloat16)
    down_part = jnp.dot(hidden, w_down, preferred_element_type=jnp.float32)
    down_chunks = down_part.reshape(row_total, count_blk, col_count).transpose(1, 0, 2)
    down_cols = scatter_axis(down_chunks, count_blk, BLK_GROUPS_UP, sum_parts)
    layer_rows = (residual + down_cols).astype(jnp.bfloat16)
    return (layer_rows.reshape(count_req, NEW, col_count), new_keys_out, new_values_out)


def solution(mesh):
    return jax.shard_map(
        body,
        mesh=mesh,
        in_specs=(
            P("req", None, None),
            P(),
            P(),
            P(),
            P(),
            P(None, "blk"),
            P(None, "blk"),
            P(None, "blk"),
            P("blk"),
            P("blk"),
            P("blk"),
            P("req", "blk", None),
            P("req", "blk", None),
            P(None, "blk"),
            P(),
            P(),
            P(None, "blk"),
            P(None, "blk"),
            P("blk", None),
        ),
        out_specs=(P("req", None, "blk"), P("req", None, "blk"), P("req", None, "blk")),
        check_vma=False,
    )
```

```python
import math

import jax
import jax.numpy as jnp
from jax import lax
from jax.sharding import PartitionSpec as P

D = 2048
HEADS = 32
HEAD_DIM = 64
ROT = 16
NEW = 4


def layer_norm(values, norm_gain, norm_bias):
    average = jnp.mean(values, -1, keepdims=True)
    centered = values - average
    variance = jnp.mean(centered * centered, -1, keepdims=True)
    return centered * lax.rsqrt(variance + 1e-05) * norm_gain + norm_bias


def rotate(heads, positions):
    half_rot = ROT // 2
    frequency = 10000.0 ** (-2.0 * jnp.arange(half_rot, dtype=jnp.float32) / ROT)
    angles = positions.astype(jnp.float32)[..., None, None] * frequency
    cosine = jnp.cos(angles)
    sine = jnp.sin(angles)
    leading = heads[..., :half_rot]
    second = heads[..., half_rot:ROT]
    unrotated = heads[..., ROT:]
    return jnp.concatenate(
        [leading * cosine - second * sine, second * cosine + leading * sine, unrotated], -1
    )


BLK_GROUPS_UP = ((0, 1), (2, 3), (4, 5))
BLK_GROUPS_DOWN = ((4, 5), (2, 3), (0, 1))


def bit_of(index, bit):
    return (index // (1 << bit)) % 2


def group_digit(index, bits):
    return sum(bit_of(index, bit) * (1 << place) for place, bit in enumerate(bits))


def group_offset(step, bits):
    return sum(((step >> place) & 1) << bit for place, bit in enumerate(bits))


def exchange(value, axis_name, count, offset):
    return lax.ppermute(value, axis_name, [(i, i ^ offset) for i in range(count)])


def fit_groups(groups, count):
    bits = count.bit_length() - 1
    kept = tuple(tuple(b for b in group if b < bits) for group in groups)
    kept = tuple(group for group in kept if group)
    covered = sorted(b for group in kept for b in group)
    if covered != list(range(bits)):
        kept = tuple((b,) for b in range(bits))
    return kept


def lane_dense(shape):
    size = math.prod(shape)
    return (size // 128, 128) if size % 128 == 0 else shape


def gather_axis(part, count, groups, axis_name="blk"):
    index = lax.axis_index(axis_name)
    bits = count.bit_length() - 1
    shape = part.shape
    part = part.reshape(lane_dense(shape))
    buffer = part
    labels = []
    for group in fit_groups(groups, count):
        size = 1 << len(group)
        digit = group_digit(index, group)
        received = [buffer]
        for step in range(1, size):
            received.append(exchange(buffer, axis_name, count, group_offset(step, group)))
        stacked = jnp.stack(received)
        buffer = jnp.take(stacked, jnp.arange(size, dtype=jnp.int32) ^ digit, axis=0)
        labels = list(reversed(group)) + labels
    buffer = buffer.reshape((2,) * bits + part.shape)
    axes = [labels.index(b) for b in range(bits - 1, -1, -1)]
    axes += list(range(bits, bits + part.ndim))
    return buffer.transpose(axes).reshape((count,) + shape)


def sum_parts(parts):
    result = parts[0]
    for part in parts[1:]:
        result = result + part
    return result


def merge_parts(parts):
    width = parts[0].shape[-1] - 2
    peak = parts[0][..., width]
    for part in parts[1:]:
        peak = jnp.maximum(peak, part[..., width])
    merged = None
    for part in parts:
        scaled = part[..., :width] * jnp.exp(part[..., width] - peak)[..., None]
        total = part[..., width + 1 :] * jnp.exp(part[..., width] - peak)[..., None]
        both = jnp.concatenate([scaled, total], -1)
        merged = both if merged is None else merged + both
    return jnp.concatenate([merged[..., :width], peak[..., None], merged[..., width:]], -1)


def scatter_axis(chunks, count, groups, combine, axis_name="blk", dense=False):
    index = lax.axis_index(axis_name)
    bits = count.bit_length() - 1
    shape = chunks.shape[1:]
    if dense:
        chunks = chunks.reshape((count,) + lane_dense(shape))
    rest = chunks.shape[1:]
    buffer = chunks.reshape((2,) * bits + rest)
    labels = list(range(bits - 1, -1, -1))
    for group in fit_groups(groups, count):
        size = 1 << len(group)
        lead = [labels.index(b) for b in reversed(group)]
        others = [axis for axis in range(len(labels)) if axis not in lead]
        buffer = buffer.transpose(lead + others + list(range(len(labels), buffer.ndim)))
        labels = [labels[axis] for axis in others]
        buffer = buffer.reshape((size,) + buffer.shape[len(group) :])
        digit = group_digit(index, group)
        parts = [lax.dynamic_index_in_dim(buffer, digit, 0, keepdims=False)]
        for step in range(1, size):
            send = lax.dynamic_index_in_dim(buffer, digit ^ step, 0, keepdims=False)
            parts.append(exchange(send, axis_name, count, group_offset(step, group)))
        buffer = combine(parts)
    return buffer.reshape(shape)


def body(
    tokens,
    lengths,
    slot_request,
    ln1_gain,
    ln1_bias,
    w_query,
    w_key,
    w_value,
    b_query,
    b_key,
    b_value,
    cache_keys,
    cache_values,
    w_out,
    ln2_gain,
    ln2_bias,
    w_gate,
    w_up,
    w_down,
):
    group_index = lax.axis_index("req")
    block_index = lax.axis_index("blk")
    count_req = tokens.shape[0]
    block_len = cache_keys.shape[1]
    col_count = w_query.shape[1]
    row_total = count_req * NEW
    column_start = block_index * col_count
    count_group = slot_request.shape[0] // count_req
    gathered = gather_axis(
        tokens, count_group, (tuple(range(count_group.bit_length() - 1)),), "req"
    ).reshape((count_group * count_req,) + tokens.shape[1:])
    owned_slots = lax.dynamic_slice_in_dim(slot_request, group_index * count_req, count_req)
    keys_by_dim = jnp.swapaxes(cache_keys, 1, 2)
    values_by_dim = jnp.swapaxes(cache_values, 1, 2)
    gathered, keys_by_dim, values_by_dim = lax.optimization_barrier(
        (gathered, keys_by_dim, values_by_dim)
    )
    inputs = jnp.take(gathered, owned_slots, axis=0).astype(jnp.float32)
    span_lengths = jnp.take(lengths, owned_slots)
    token_rows = inputs.reshape(row_total, D)
    normed = layer_norm(token_rows, ln1_gain, ln1_bias).astype(jnp.bfloat16)
    query_cols = (jnp.dot(normed, w_query, preferred_element_type=jnp.float32) + b_query).astype(
        jnp.bfloat16
    )
    key_cols = (jnp.dot(normed, w_key, preferred_element_type=jnp.float32) + b_key).astype(
        jnp.bfloat16
    )
    value_cols = (jnp.dot(normed, w_value, preferred_element_type=jnp.float32) + b_value).astype(
        jnp.bfloat16
    )
    count_blk = D // col_count
    packed = jnp.concatenate([query_cols, key_cols, value_cols], 1)
    gathered_cols = gather_axis(packed, count_blk, BLK_GROUPS_DOWN)
    whole_cols = gathered_cols.transpose(1, 0, 2)
    query_raw = whole_cols[:, :, :col_count].reshape(row_total, D)
    key_raw = whole_cols[:, :, col_count : 2 * col_count].reshape(row_total, D)
    value_raw = whole_cols[:, :, 2 * col_count :].reshape(row_total, D)
    positions = span_lengths[:, None] + jnp.arange(NEW, dtype=jnp.int32)[None, :]
    head_shape = (count_req, NEW, HEADS, HEAD_DIM)
    queries = rotate(query_raw.astype(jnp.float32).reshape(head_shape), positions).astype(
        jnp.bfloat16
    )
    keys_new = rotate(key_raw.astype(jnp.float32).reshape(head_shape), positions).astype(
        jnp.bfloat16
    )
    values_new = value_raw.reshape(head_shape)
    new_keys_out = lax.dynamic_slice_in_dim(
        keys_new.reshape(count_req, NEW, D), column_start, col_count, 2
    )
    new_values_out = lax.dynamic_slice_in_dim(
        value_raw.reshape(count_req, NEW, D), column_start, col_count, 2
    )
    score_scale = HEAD_DIM ** (-0.5)
    key_heads = keys_by_dim.reshape(count_req, HEADS, HEAD_DIM, block_len)
    value_heads = values_by_dim.reshape(count_req, HEADS, HEAD_DIM, block_len)
    scores = (
        jnp.einsum("rthd,rhdp->rthp", queries, key_heads, preferred_element_type=jnp.float32)
        * score_scale
    )
    places = block_index * block_len + jnp.arange(block_len, dtype=jnp.int32)
    visible = places[None, None, None, :] < span_lengths[:, None, None, None]
    peak_local = jnp.max(jnp.where(visible, scores, -1e30), -1)
    weights = jnp.where(visible, jnp.exp(scores - peak_local[..., None]), 0.0)
    total_local = jnp.sum(weights, -1)
    accum_local = jnp.einsum(
        "rthp,rhdp->rthd",
        weights.astype(jnp.bfloat16),
        value_heads,
        preferred_element_type=jnp.float32,
    )
    fresh_scores = (
        jnp.einsum("rthd,rshd->rths", queries, keys_new, preferred_element_type=jnp.float32)
        * score_scale
    )
    causal = jnp.arange(NEW)[:, None, None] >= jnp.arange(NEW)[None, None, :]
    fresh_peak = jnp.max(jnp.where(causal, fresh_scores, -1e30), -1)
    fresh_weights = jnp.where(causal, jnp.exp(fresh_scores - fresh_peak[..., None]), 0.0)
    fresh_total = jnp.sum(fresh_weights, -1)
    fresh_accum = jnp.einsum(
        "rths,rshd->rthd",
        fresh_weights.astype(jnp.bfloat16),
        values_new,
        preferred_element_type=jnp.float32,
    )
    head_rows = row_total * HEADS
    share = head_rows // count_blk
    packed_rows = jnp.concatenate(
        [
            accum_local.reshape(head_rows, HEAD_DIM),
            peak_local.reshape(head_rows, 1),
            total_local.reshape(head_rows, 1),
        ],
        -1,
    ).reshape(count_blk, share, HEAD_DIM + 2)
    merged = scatter_axis(packed_rows, count_blk, BLK_GROUPS_UP, merge_parts)
    cache_accum = merged[:, :HEAD_DIM]
    cache_peak = merged[:, HEAD_DIM]
    cache_total = merged[:, HEAD_DIM + 1]
    row_start = block_index * share
    fresh_peak_own = lax.dynamic_slice_in_dim(fresh_peak.reshape(head_rows), row_start, share)
    fresh_total_own = lax.dynamic_slice_in_dim(fresh_total.reshape(head_rows), row_start, share)
    fresh_accum_own = lax.dynamic_slice_in_dim(
        fresh_accum.reshape(head_rows, HEAD_DIM), row_start, share
    )
    peak_all = jnp.maximum(cache_peak, fresh_peak_own)
    scale_cache = jnp.exp(cache_peak - peak_all)
    scale_new = jnp.exp(fresh_peak_own - peak_all)
    numer = cache_accum * scale_cache[:, None] + fresh_accum_own * scale_new[:, None]
    denom = cache_total * scale_cache + fresh_total_own * scale_new
    attended_own = (numer / denom[:, None]).astype(jnp.bfloat16)
    attended = gather_axis(attended_own, count_blk, BLK_GROUPS_DOWN).reshape(row_total, D)
    input_cols = lax.dynamic_slice_in_dim(token_rows, column_start, col_count, 1)
    residual = input_cols + jnp.dot(attended, w_out, preferred_element_type=jnp.float32)
    gathered_rows = gather_axis(residual.astype(jnp.bfloat16), count_blk, BLK_GROUPS_DOWN)
    whole_rows = gathered_rows.transpose(1, 0, 2).reshape(row_total, D).astype(jnp.float32)
    normed_two = layer_norm(whole_rows, ln2_gain, ln2_bias).astype(jnp.bfloat16)
    gate_proj = jnp.dot(normed_two, w_gate, preferred_element_type=jnp.float32)
    up_proj = jnp.dot(normed_two, w_up, preferred_element_type=jnp.float32)
    hidden = (jax.nn.silu(gate_proj) * up_proj).astype(jnp.bfloat16)
    down_part = jnp.dot(hidden, w_down, preferred_element_type=jnp.float32)
    down_chunks = down_part.reshape(row_total, count_blk, col_count).transpose(1, 0, 2)
    down_cols = scatter_axis(down_chunks, count_blk, BLK_GROUPS_UP, sum_parts, dense=True)
    layer_rows = (residual + down_cols).astype(jnp.bfloat16)
    return (layer_rows.reshape(count_req, NEW, col_count), new_keys_out, new_values_out)


def solution(mesh):
    return jax.shard_map(
        body,
        mesh=mesh,
        in_specs=(
            P("req", None, None),
            P(),
            P(),
            P(),
            P(),
            P(None, "blk"),
            P(None, "blk"),
            P(None, "blk"),
            P("blk"),
            P("blk"),
            P("blk"),
            P("req", "blk", None),
            P("req", "blk", None),
            P(None, "blk"),
            P(),
            P(),
            P(None, "blk"),
            P(None, "blk"),
            P("blk", None),
        ),
        out_specs=(P("req", None, "blk"), P("req", None, "blk"), P("req", None, "blk")),
        check_vma=False,
    )
```

```python
import math

import jax
import jax.numpy as jnp
from jax import lax
from jax.sharding import PartitionSpec as P

D = 2048
HEADS = 32
HEAD_DIM = 64
ROT = 16
NEW = 4


def layer_norm(values, norm_gain, norm_bias):
    average = jnp.mean(values, -1, keepdims=True)
    centered = values - average
    variance = jnp.mean(centered * centered, -1, keepdims=True)
    return centered * lax.rsqrt(variance + 1e-05) * norm_gain + norm_bias


def rotate(heads, positions):
    half_rot = ROT // 2
    frequency = 10000.0 ** (-2.0 * jnp.arange(half_rot, dtype=jnp.float32) / ROT)
    angles = positions.astype(jnp.float32)[..., None, None] * frequency
    cosine = jnp.cos(angles)
    sine = jnp.sin(angles)
    leading = heads[..., :half_rot]
    second = heads[..., half_rot:ROT]
    unrotated = heads[..., ROT:]
    return jnp.concatenate(
        [leading * cosine - second * sine, second * cosine + leading * sine, unrotated], -1
    )


BLK_GROUPS_UP = ((0, 1), (2, 3), (4, 5))
BLK_GROUPS_DOWN = ((4, 5), (2, 3), (0, 1))


def bit_of(index, bit):
    return (index // (1 << bit)) % 2


def group_digit(index, bits):
    return sum(bit_of(index, bit) * (1 << place) for place, bit in enumerate(bits))


def group_offset(step, bits):
    return sum(((step >> place) & 1) << bit for place, bit in enumerate(bits))


def exchange(value, axis_name, count, offset):
    return lax.ppermute(value, axis_name, [(i, i ^ offset) for i in range(count)])


def fit_groups(groups, count):
    bits = count.bit_length() - 1
    kept = tuple(tuple(b for b in group if b < bits) for group in groups)
    kept = tuple(group for group in kept if group)
    covered = sorted(b for group in kept for b in group)
    if covered != list(range(bits)):
        kept = tuple((b,) for b in range(bits))
    return kept


def lane_dense(shape):
    size = math.prod(shape)
    return (size // 128, 128) if size % 128 == 0 else shape


def gather_axis(part, count, groups, axis_name="blk"):
    index = lax.axis_index(axis_name)
    bits = count.bit_length() - 1
    shape = part.shape
    part = part.reshape(lane_dense(shape))
    buffer = part
    labels = []
    for group in fit_groups(groups, count):
        size = 1 << len(group)
        digit = group_digit(index, group)
        received = [buffer]
        for step in range(1, size):
            received.append(exchange(buffer, axis_name, count, group_offset(step, group)))
        stacked = jnp.stack(received)
        buffer = jnp.take(stacked, jnp.arange(size, dtype=jnp.int32) ^ digit, axis=0)
        labels = list(reversed(group)) + labels
    buffer = buffer.reshape((2,) * bits + part.shape)
    axes = [labels.index(b) for b in range(bits - 1, -1, -1)]
    axes += list(range(bits, bits + part.ndim))
    return buffer.transpose(axes).reshape((count,) + shape)


def sum_parts(parts):
    result = parts[0]
    for part in parts[1:]:
        result = result + part
    return result


def merge_parts(parts):
    width = parts[0].shape[-1] - 2
    peak = parts[0][..., width]
    for part in parts[1:]:
        peak = jnp.maximum(peak, part[..., width])
    merged = None
    for part in parts:
        scaled = part[..., :width] * jnp.exp(part[..., width] - peak)[..., None]
        total = part[..., width + 1 :] * jnp.exp(part[..., width] - peak)[..., None]
        both = jnp.concatenate([scaled, total], -1)
        merged = both if merged is None else merged + both
    return jnp.concatenate([merged[..., :width], peak[..., None], merged[..., width:]], -1)


def scatter_axis(chunks, count, groups, combine, axis_name="blk", dense=False, wire=None):
    index = lax.axis_index(axis_name)
    bits = count.bit_length() - 1
    shape = chunks.shape[1:]
    if dense:
        chunks = chunks.reshape((count,) + lane_dense(shape))
    rest = chunks.shape[1:]
    buffer = chunks.reshape((2,) * bits + rest)
    labels = list(range(bits - 1, -1, -1))
    for group in fit_groups(groups, count):
        size = 1 << len(group)
        lead = [labels.index(b) for b in reversed(group)]
        others = [axis for axis in range(len(labels)) if axis not in lead]
        buffer = buffer.transpose(lead + others + list(range(len(labels), buffer.ndim)))
        labels = [labels[axis] for axis in others]
        buffer = buffer.reshape((size,) + buffer.shape[len(group) :])
        digit = group_digit(index, group)
        parts = [lax.dynamic_index_in_dim(buffer, digit, 0, keepdims=False)]
        for step in range(1, size):
            send = lax.dynamic_index_in_dim(buffer, digit ^ step, 0, keepdims=False)
            sent = send if wire is None else send.astype(wire)
            got = exchange(sent, axis_name, count, group_offset(step, group))
            parts.append(got.astype(send.dtype))
        buffer = combine(parts)
    return buffer.reshape(shape)


def body(
    tokens,
    lengths,
    slot_request,
    ln1_gain,
    ln1_bias,
    w_query,
    w_key,
    w_value,
    b_query,
    b_key,
    b_value,
    cache_keys,
    cache_values,
    w_out,
    ln2_gain,
    ln2_bias,
    w_gate,
    w_up,
    w_down,
):
    group_index = lax.axis_index("req")
    block_index = lax.axis_index("blk")
    count_req = tokens.shape[0]
    block_len = cache_keys.shape[1]
    col_count = w_query.shape[1]
    row_total = count_req * NEW
    column_start = block_index * col_count
    count_group = slot_request.shape[0] // count_req
    gathered = gather_axis(
        tokens, count_group, (tuple(range(count_group.bit_length() - 1)),), "req"
    ).reshape((count_group * count_req,) + tokens.shape[1:])
    owned_slots = lax.dynamic_slice_in_dim(slot_request, group_index * count_req, count_req)
    keys_by_dim = jnp.swapaxes(cache_keys, 1, 2)
    values_by_dim = jnp.swapaxes(cache_values, 1, 2)
    gathered, keys_by_dim, values_by_dim = lax.optimization_barrier(
        (gathered, keys_by_dim, values_by_dim)
    )
    inputs = jnp.take(gathered, owned_slots, axis=0).astype(jnp.float32)
    span_lengths = jnp.take(lengths, owned_slots)
    token_rows = inputs.reshape(row_total, D)
    normed = layer_norm(token_rows, ln1_gain, ln1_bias).astype(jnp.bfloat16)
    query_cols = (jnp.dot(normed, w_query, preferred_element_type=jnp.float32) + b_query).astype(
        jnp.bfloat16
    )
    key_cols = (jnp.dot(normed, w_key, preferred_element_type=jnp.float32) + b_key).astype(
        jnp.bfloat16
    )
    value_cols = (jnp.dot(normed, w_value, preferred_element_type=jnp.float32) + b_value).astype(
        jnp.bfloat16
    )
    count_blk = D // col_count
    packed = jnp.concatenate([query_cols, key_cols, value_cols], 1)
    gathered_cols = gather_axis(packed, count_blk, BLK_GROUPS_DOWN)
    whole_cols = gathered_cols.transpose(1, 0, 2)
    query_raw = whole_cols[:, :, :col_count].reshape(row_total, D)
    key_raw = whole_cols[:, :, col_count : 2 * col_count].reshape(row_total, D)
    value_raw = whole_cols[:, :, 2 * col_count :].reshape(row_total, D)
    positions = span_lengths[:, None] + jnp.arange(NEW, dtype=jnp.int32)[None, :]
    head_shape = (count_req, NEW, HEADS, HEAD_DIM)
    queries = rotate(query_raw.astype(jnp.float32).reshape(head_shape), positions).astype(
        jnp.bfloat16
    )
    keys_new = rotate(key_raw.astype(jnp.float32).reshape(head_shape), positions).astype(
        jnp.bfloat16
    )
    values_new = value_raw.reshape(head_shape)
    new_keys_out = lax.dynamic_slice_in_dim(
        keys_new.reshape(count_req, NEW, D), column_start, col_count, 2
    )
    new_values_out = lax.dynamic_slice_in_dim(
        value_raw.reshape(count_req, NEW, D), column_start, col_count, 2
    )
    score_scale = HEAD_DIM ** (-0.5)
    key_heads = keys_by_dim.reshape(count_req, HEADS, HEAD_DIM, block_len)
    value_heads = values_by_dim.reshape(count_req, HEADS, HEAD_DIM, block_len)
    scores = (
        jnp.einsum("rthd,rhdp->rthp", queries, key_heads, preferred_element_type=jnp.float32)
        * score_scale
    )
    places = block_index * block_len + jnp.arange(block_len, dtype=jnp.int32)
    visible = places[None, None, None, :] < span_lengths[:, None, None, None]
    peak_local = jnp.max(jnp.where(visible, scores, -1e30), -1)
    weights = jnp.where(visible, jnp.exp(scores - peak_local[..., None]), 0.0)
    total_local = jnp.sum(weights, -1)
    accum_local = jnp.einsum(
        "rthp,rhdp->rthd",
        weights.astype(jnp.bfloat16),
        value_heads,
        preferred_element_type=jnp.float32,
    )
    fresh_scores = (
        jnp.einsum("rthd,rshd->rths", queries, keys_new, preferred_element_type=jnp.float32)
        * score_scale
    )
    causal = jnp.arange(NEW)[:, None, None] >= jnp.arange(NEW)[None, None, :]
    fresh_peak = jnp.max(jnp.where(causal, fresh_scores, -1e30), -1)
    fresh_weights = jnp.where(causal, jnp.exp(fresh_scores - fresh_peak[..., None]), 0.0)
    fresh_total = jnp.sum(fresh_weights, -1)
    fresh_accum = jnp.einsum(
        "rths,rshd->rthd",
        fresh_weights.astype(jnp.bfloat16),
        values_new,
        preferred_element_type=jnp.float32,
    )
    head_rows = row_total * HEADS
    share = head_rows // count_blk
    packed_rows = jnp.concatenate(
        [
            accum_local.reshape(head_rows, HEAD_DIM),
            peak_local.reshape(head_rows, 1),
            total_local.reshape(head_rows, 1),
        ],
        -1,
    ).reshape(count_blk, share, HEAD_DIM + 2)
    merged = scatter_axis(packed_rows, count_blk, BLK_GROUPS_UP, merge_parts)
    cache_accum = merged[:, :HEAD_DIM]
    cache_peak = merged[:, HEAD_DIM]
    cache_total = merged[:, HEAD_DIM + 1]
    row_start = block_index * share
    fresh_peak_own = lax.dynamic_slice_in_dim(fresh_peak.reshape(head_rows), row_start, share)
    fresh_total_own = lax.dynamic_slice_in_dim(fresh_total.reshape(head_rows), row_start, share)
    fresh_accum_own = lax.dynamic_slice_in_dim(
        fresh_accum.reshape(head_rows, HEAD_DIM), row_start, share
    )
    peak_all = jnp.maximum(cache_peak, fresh_peak_own)
    scale_cache = jnp.exp(cache_peak - peak_all)
    scale_new = jnp.exp(fresh_peak_own - peak_all)
    numer = cache_accum * scale_cache[:, None] + fresh_accum_own * scale_new[:, None]
    denom = cache_total * scale_cache + fresh_total_own * scale_new
    attended_own = (numer / denom[:, None]).astype(jnp.bfloat16)
    attended = gather_axis(attended_own, count_blk, BLK_GROUPS_DOWN).reshape(row_total, D)
    input_cols = lax.dynamic_slice_in_dim(token_rows, column_start, col_count, 1)
    residual = input_cols + jnp.dot(attended, w_out, preferred_element_type=jnp.float32)
    gathered_rows = gather_axis(residual.astype(jnp.bfloat16), count_blk, BLK_GROUPS_DOWN)
    whole_rows = gathered_rows.transpose(1, 0, 2).reshape(row_total, D).astype(jnp.float32)
    normed_two = layer_norm(whole_rows, ln2_gain, ln2_bias).astype(jnp.bfloat16)
    gate_proj = jnp.dot(normed_two, w_gate, preferred_element_type=jnp.float32)
    up_proj = jnp.dot(normed_two, w_up, preferred_element_type=jnp.float32)
    hidden = (jax.nn.silu(gate_proj) * up_proj).astype(jnp.bfloat16)
    down_part = jnp.dot(hidden, w_down, preferred_element_type=jnp.float32)
    down_chunks = down_part.reshape(row_total, count_blk, col_count).transpose(1, 0, 2)
    down_cols = scatter_axis(
        down_chunks, count_blk, BLK_GROUPS_UP, sum_parts, dense=True, wire=jnp.bfloat16
    )
    layer_rows = (residual + down_cols).astype(jnp.bfloat16)
    return (layer_rows.reshape(count_req, NEW, col_count), new_keys_out, new_values_out)


def solution(mesh):
    return jax.shard_map(
        body,
        mesh=mesh,
        in_specs=(
            P("req", None, None),
            P(),
            P(),
            P(),
            P(),
            P(None, "blk"),
            P(None, "blk"),
            P(None, "blk"),
            P("blk"),
            P("blk"),
            P("blk"),
            P("req", "blk", None),
            P("req", "blk", None),
            P(None, "blk"),
            P(),
            P(),
            P(None, "blk"),
            P(None, "blk"),
            P("blk", None),
        ),
        out_specs=(P("req", None, "blk"), P("req", None, "blk"), P("req", None, "blk")),
        check_vma=False,
    )
```
